256 devices in a mesh: tm: 4 (over y), row: 4 (over x), col: 16 (over z, core).
Axes of the slice: x: 4, y: 4, z: 8, core: 2. Of those that a mesh axis runs over, the one named last changes fastest.
Arguments:
- day_block: float32 [4, 4, 16, 32, 4, 4, 128], P('tm', None, 'col', None, None, 'row'), as said below
- left_coupling: float32 [4, 4, 16, 32, 4, 4, 128], P('tm', None, 'col', None, None, 'row'), may hold values from -0.125 to 0.125
- right_coupling: float32 [4, 4, 16, 32, 4, 4, 128], P('tm', None, 'col', None, None, 'row'), may hold values from -0.125 to 0.125
- separator_block: float32 [4, 4, 16, 32, 4, 4, 128], P('tm', None, 'col', None, None, 'row')
- arrow_coupling: float32 [4, 4, 16, 32, 64], P('tm', None, 'col'), may hold values from -0.125 to 0.125
- arrow_block: float32 [64, 64], replicated
Outputs:
- day_factor: float32 [4, 4, 16, 32, 4, 4, 128], P('tm', None, 'col', None, None, 'row')
- left_factor: float32 [4, 4, 16, 32, 4, 4, 128], P('tm', None, 'col', None, None, 'row')
- right_factor: float32 [4, 4, 16, 32, 4, 4, 128], P('tm', None, 'col', None, None, 'row')
- arrow_factor: float32 [4, 4, 16, 32, 64], P('tm', None, 'col')
- separator: float32 [4, 4, 16, 32, 4, 4, 128], P('tm', None, 'col', None, None, 'row')
- arrowhead: float32 [64, 64], replicated
The draws below stay inside these ranges and needn't reach their ends.
Inputs may be any that keep to these rules, and one draw needn't show every extreme that they name: Each group's day_block and separator_block, and arrow_block, is an exactly symmetric matrix with all eigenvalues at least 1.
All inputs are finite; a program needn't handle non-finite values.
Results may differ from the reference program's by a relative error of at most 0.0001.
Values sent between devices are 32-bit elements; how exact they have to be, the bound alone decides.
No kernel may reach another device: no remote copies, remote signals or barrier semaphores. Data moves between devices by JAX's collectives and lax.ppermute only.
A program may use at most 128 MiB of HBM per device.

```python
import jax
import jax.numpy as jnp
from jax import lax

N = 2048
P_SIZE = 512
ARW = 64
GROUPS = 4
NP = 4
PC = 32
PR = 128
N_ROW = 4
N_COL = 16


def definite_matrix(key, order):
    first_key, second_key = jax.random.split(key)
    base = jax.random.normal(first_key, (order, order), jnp.float32)
    diagonal = jax.random.uniform(second_key, (order,), jnp.float32, 1.0, 3.0)
    gram = jnp.dot(base, base.T, precision=lax.Precision.HIGHEST) / order
    return 0.5 * (gram + gram.T) + jnp.diag(diagonal)


def group_matrices(key):
    keys = jax.random.split(key, GROUPS)
    stacked = jnp.stack([definite_matrix(keys[group], N) for group in range(GROUPS)])
    return stacked.reshape(GROUPS, NP, P_SIZE // PC, PC, NP, P_SIZE // PR, PR)


def draw_day_block(key, part):
    return group_matrices(jax.random.fold_in(key, 11))


def draw_separator_block(key, part):
    return group_matrices(jax.random.fold_in(key, 23))


def draw_arrow_block(key, part):
    return definite_matrix(jax.random.fold_in(key, 37), ARW)


def block_scale(key, shape, pieces, low, largest):
    factor_of, own = 1.0, jax.random.fold_in(key, 6)
    for dim, parts in pieces:
        steps = jnp.exp(jax.random.uniform(jax.random.fold_in(own, dim), (parts,), jnp.float32, low / len(pieces), largest / len(pieces)))
        factor_of = factor_of * jnp.repeat(steps, shape[dim] // parts).reshape([-1 if axis == dim else 1 for axis in range(len(shape))])
    return factor_of


def scatter_about(rng, extent, spread, most, pieces=(), held_as=jnp.bfloat16):
    result = jax.random.normal(rng, extent, jnp.float32) * spread
    if len(pieces) > 0:
        result = block_scale(rng, extent, pieces, -0.22, 0.18) * result
    return jnp.clip(result, min=-most, max=most).astype(held_as)


def setup_inputs(seed: int = 0) -> dict:
    seeds = jax.random.split(jax.random.key(seed), 7)
    day_block = draw_day_block(jax.random.fold_in(seeds[6], 71), 0)
    left_coupling = scatter_about(seeds[1], (GROUPS, NP, N_COL, PC, NP, N_ROW, PR), N ** -0.5, 0.125, ((0, 4), (2, 16), (5, 4)), jnp.float32)
    right_coupling = scatter_about(seeds[2], (GROUPS, NP, N_COL, PC, NP, N_ROW, PR), N ** -0.5, 0.125, ((0, 4), (2, 16), (5, 4)), jnp.float32)
    separator_block = draw_separator_block(jax.random.fold_in(seeds[6], 71), 0)
    arrow_coupling = scatter_about(seeds[4], (GROUPS, NP, N_COL, PC, ARW), N ** -0.5, 0.125, ((0, 4), (2, 16)), jnp.float32)
    arrow_block = draw_arrow_block(jax.random.fold_in(seeds[6], 71), 0)
    return dict(day_block=day_block, left_coupling=left_coupling, right_coupling=right_coupling, separator_block=separator_block, arrow_coupling=arrow_coupling, arrow_block=arrow_block)


def product(left, right):
    return jnp.dot(left.astype(jnp.float32), right.astype(jnp.float32), precision=lax.Precision.HIGHEST, preferred_element_type=jnp.float32)

def lower_solve(factor, right):
    return lax.linalg.triangular_solve(factor, right, left_side=True, lower=True)

def reference(day_block, left_coupling, right_coupling, separator_block, arrow_coupling, arrow_block):
    groups = day_block.shape[0]
    shape_big = day_block.shape[1:]
    shape_arrow = arrow_coupling.shape[1:]
    factors = []
    lefts = []
    rights = []
    arrows = []
    for group in range(groups):
        lower = jnp.linalg.cholesky(day_block[group].reshape(N, N))
        factors.append(lower.T)
        lefts.append(lower_solve(lower, left_coupling[group].reshape(N, N)))
        rights.append(lower_solve(lower, right_coupling[group].reshape(N, N)))
        arrows.append(lower_solve(lower, arrow_coupling[group].reshape(N, ARW)))
    separators = []
    arrow_total = jnp.zeros((ARW, ARW), jnp.float32)
    for group in range(groups):
        update = separator_block[group].reshape(N, N) - product(rights[group].T, rights[group])
        if group + 1 < groups:
            update = update - product(lefts[group + 1].T, lefts[group + 1])
        separators.append(update.reshape(shape_big))
        arrow_total = arrow_total + product(arrows[group].T, arrows[group])
    day_factor = jnp.stack([item.reshape(shape_big) for item in factors])
    left_factor = jnp.stack([item.reshape(shape_big) for item in lefts])
    right_factor = jnp.stack([item.reshape(shape_big) for item in rights])
    arrow_factor = jnp.stack([item.reshape(shape_arrow) for item in arrows])
    separator = jnp.stack(separators)
    arrowhead = arrow_block - arrow_total
    return (day_factor, left_factor, right_factor, arrow_factor, separator, arrowhead)
```

```python
import jax
import jax.numpy as jnp
from jax import lax
from jax.sharding import PartitionSpec as P


def passed_along(value, axis, steps):
    count = lax.axis_size(axis)
    initial, last = (max(0, -steps), min(count, count - steps))
    return lax.ppermute(value, axis, [(source, source + steps) for source in range(initial, last)])


def product(left, right):
    return jnp.dot(left, right, precision=lax.Precision.HIGHEST, preferred_element_type=jnp.float32)


def lower_inverse(factor):
    identity = jnp.eye(factor.shape[0], dtype=jnp.float32)
    return lax.linalg.triangular_solve(factor, identity, left_side=True, lower=True)


def reorder_nodes(whole, panels, col_width):
    count = whole.shape[0]
    col_count = lax.axis_size("col")
    spread = whole.reshape(count, panels, col_count, col_width)
    return jnp.transpose(spread, (2, 1, 3, 0)).reshape(col_count * panels * col_width, count)


def separator_term(solved, panels, col_width, row_width):
    whole = lax.all_gather(
        solved.reshape(solved.shape[0], panels, 1, row_width), "row", axis=2, tiled=True
    )
    ordered = reorder_nodes(whole, panels, col_width)
    return lax.psum_scatter(product(ordered, solved), "col", scatter_dimension=0, tiled=True)


def per_device(
    day_block, left_coupling, right_coupling, separator_block, arrow_coupling, arrow_block
):
    panels = day_block.shape[1]
    col_width = day_block.shape[3]
    row_width = day_block.shape[6]
    panel_size = col_width * lax.axis_size("col")
    arrow_rows = arrow_block.shape[0]
    col_index = lax.axis_index("col")
    row_index = lax.axis_index("row")
    matrix = day_block.reshape(panels, col_width, panels, row_width)
    left_part = left_coupling.reshape(panels, col_width, panels, row_width)
    right_part = right_coupling.reshape(panels, col_width, panels, row_width)
    arrow_part = arrow_coupling.reshape(panels, col_width, arrow_rows)
    rows_at = col_index * col_width + lax.broadcasted_iota(jnp.int32, (col_width, row_width), 0)
    cols_at = row_index * row_width + lax.broadcasted_iota(jnp.int32, (col_width, row_width), 1)
    factor_blocks = []
    left_blocks = []
    right_blocks = []
    arrow_blocks = []
    for current in range(panels):
        remain = panels - current
        gathered_day, gathered_left, gathered_right, gathered_arrow = (
            lax.all_gather(matrix[current, :, current:, :], "col", axis=0, tiled=True),
            lax.all_gather(left_part[current], "col", axis=0, tiled=True),
            lax.all_gather(right_part[current], "col", axis=0, tiled=True),
            lax.all_gather(arrow_part[current], "col", axis=0, tiled=True),
        )
        diagonal_full = lax.all_gather(gathered_day[:, 0:1, :], "row", axis=1, tiled=True).reshape(
            panel_size, panel_size
        )
        factor = jnp.linalg.cholesky(diagonal_full)
        inverse = lower_inverse(factor)
        owned = product(inverse, gathered_day.reshape(panel_size, remain * row_width)).reshape(
            panel_size, remain, row_width
        )
        if remain > 1:
            later = lax.all_gather(owned[:, 1:, None, :], "row", axis=2, tiled=True).reshape(
                panel_size, remain - 1, panel_size
            )
        solved_left = product(inverse, gathered_left.reshape(panel_size, panels * row_width))
        solved_right = product(inverse, gathered_right.reshape(panel_size, panels * row_width))
        solved_arrow = product(inverse, gathered_arrow)
        mine_rows = lax.dynamic_slice_in_dim(owned, col_index * col_width, col_width, 0)
        diagonal_part = jnp.where(cols_at >= rows_at, mine_rows[:, 0, :], 0.0)
        factor_blocks.append(
            jnp.concatenate(
                [
                    jnp.zeros((col_width, current, row_width), jnp.float32),
                    diagonal_part[:, None, :],
                    mine_rows[:, 1:, :],
                ],
                axis=1,
            )
        )
        left_blocks.append(
            lax.dynamic_slice_in_dim(solved_left, col_index * col_width, col_width, 0)
        )
        right_blocks.append(
            lax.dynamic_slice_in_dim(solved_right, col_index * col_width, col_width, 0)
        )
        arrow_blocks.append(
            lax.dynamic_slice_in_dim(solved_arrow, col_index * col_width, col_width, 0)
        )
        if remain > 1:
            mine_later = lax.dynamic_slice_in_dim(later, col_index * col_width, col_width, 2)
            mine_later = mine_later.reshape(panel_size, (remain - 1) * col_width).T
            owned_later = owned[:, 1:, :].reshape(panel_size, (remain - 1) * row_width)
            matrix = matrix.at[current + 1 :, :, current + 1 :, :].add(
                -product(mine_later, owned_later).reshape(
                    remain - 1, col_width, remain - 1, row_width
                )
            )
            left_part = left_part.at[current + 1 :].add(
                -product(mine_later, solved_left).reshape(remain - 1, col_width, panels, row_width)
            )
            right_part = right_part.at[current + 1 :].add(
                -product(mine_later, solved_right).reshape(remain - 1, col_width, panels, row_width)
            )
            arrow_part = arrow_part.at[current + 1 :].add(
                -product(mine_later, solved_arrow).reshape(remain - 1, col_width, arrow_rows)
            )
    day_factor = jnp.stack(factor_blocks).reshape(day_block.shape)
    left_solved = jnp.stack(left_blocks).reshape(panels * col_width, panels * row_width)
    right_solved = jnp.stack(right_blocks).reshape(panels * col_width, panels * row_width)
    arrow_solved = jnp.stack(arrow_blocks).reshape(panels * col_width, arrow_rows)
    separator_local = separator_block.reshape(panels * col_width, panels * row_width)
    right_term = separator_term(right_solved, panels, col_width, row_width)
    left_term = separator_term(left_solved, panels, col_width, row_width)
    from_next = passed_along(left_term, "tm", -1)
    separator = separator_local - right_term - from_next
    arrow_local = product(arrow_solved.T, arrow_solved)
    arrow_local = jnp.where(row_index == 0, arrow_local, 0.0)
    arrow_total = lax.psum(arrow_local, ("tm", "row", "col"))
    arrowhead = arrow_block - arrow_total
    return (
        day_factor,
        left_solved.reshape(left_coupling.shape),
        right_solved.reshape(right_coupling.shape),
        arrow_solved.reshape(arrow_coupling.shape),
        separator.reshape(separator_block.shape),
        arrowhead,
    )


def solution(mesh):
    return jax.shard_map(
        per_device,
        mesh=mesh,
        in_specs=(
            P("tm", None, "col", None, None, "row", None),
            P("tm", None, "col", None, None, "row", None),
            P("tm", None, "col", None, None, "row", None),
            P("tm", None, "col", None, None, "row", None),
            P("tm", None, "col", None, None),
            P(),
        ),
        out_specs=(
            P("tm", None, "col", None, None, "row", None),
            P("tm", None, "col", None, None, "row", None),
            P("tm", None, "col", None, None, "row", None),
            P("tm", None, "col", None, None),
            P("tm", None, "col", None, None, "row", None),
            P(),
        ),
        check_vma=False,
    )
```

```python
import jax
import jax.numpy as jnp
from jax import lax
from jax.sharding import PartitionSpec as P


def passed_along(value, axis, steps):
    count = lax.axis_size(axis)
    initial, last = (max(0, -steps), min(count, count - steps))
    return lax.ppermute(value, axis, [(source, source + steps) for source in range(initial, last)])


def product(left, right):
    return jnp.dot(left, right, precision=lax.Precision.HIGHEST, preferred_element_type=jnp.float32)


def lower_inverse(factor):
    identity = jnp.eye(factor.shape[0], dtype=jnp.float32)
    return lax.linalg.triangular_solve(factor, identity, left_side=True, lower=True)


def reorder_nodes(whole, panels, col_width):
    count = whole.shape[0]
    col_count = lax.axis_size("col")
    spread = whole.reshape(count, panels, col_count, col_width)
    return jnp.transpose(spread, (2, 1, 3, 0)).reshape(col_count * panels * col_width, count)


def separator_term(solved, panels, col_width, row_width):
    whole = lax.all_gather(
        solved.reshape(solved.shape[0], panels, 1, row_width), "row", axis=2, tiled=True
    )
    ordered = reorder_nodes(whole, panels, col_width)
    return lax.psum_scatter(product(ordered, solved), "col", scatter_dimension=0, tiled=True)


def product_tn(left, right):
    return lax.dot_general(
        left,
        right,
        (((0,), (0,)), ((), ())),
        precision=lax.Precision.HIGHEST,
        preferred_element_type=jnp.float32,
    )


def per_device(
    day_block, left_coupling, right_coupling, separator_block, arrow_coupling, arrow_block
):
    panels = day_block.shape[1]
    col_width = day_block.shape[3]
    row_width = day_block.shape[6]
    col_count = lax.axis_size("col")
    row_count = lax.axis_size("row")
    panel_size = col_width * col_count
    arrow_rows = arrow_block.shape[0]
    col_index = lax.axis_index("col")
    row_index = lax.axis_index("row")
    matrix = day_block.reshape(panels, col_width, panels, row_width)
    left_part = left_coupling.reshape(panels, col_width, panels * row_width)
    right_part = right_coupling.reshape(panels, col_width, panels * row_width)
    arrow_part = arrow_coupling.reshape(panels, col_width, arrow_rows)
    left_full = [lax.all_gather(left_part[k], "col", axis=0, tiled=True) for k in range(panels)]
    right_full = [lax.all_gather(right_part[k], "col", axis=0, tiled=True) for k in range(panels)]
    arrow_full = [lax.all_gather(arrow_part[k], "col", axis=0, tiled=True) for k in range(panels)]
    rows_at = col_index * col_width + lax.broadcasted_iota(jnp.int32, (col_width, row_width), 0)
    cols_at = row_index * row_width + lax.broadcasted_iota(jnp.int32, (col_width, row_width), 1)
    per_slice = row_width // col_width
    owner = col_index // per_slice
    offset = (col_index % per_slice) * col_width

    def own_columns(solved):
        spread = solved.reshape(panel_size, panels, row_width)
        picked = lax.dynamic_slice_in_dim(spread, offset, col_width, 2)
        picked = jnp.where(row_index == owner, picked, 0.0)
        return lax.psum(picked, "row").reshape(panel_size, panels * col_width)

    factor_blocks = []
    left_solved = []
    right_solved = []
    arrow_solved = []
    right_term = jnp.zeros((panels * col_width, panels * row_width), jnp.float32)
    left_term = jnp.zeros((panels * col_width, panels * row_width), jnp.float32)
    arrow_term = jnp.zeros((arrow_rows, arrow_rows), jnp.float32)
    for current in range(panels):
        remain = panels - current
        gathered_day = lax.all_gather(matrix[current, :, current:, :], "col", axis=0, tiled=True)
        diagonal_full = lax.all_gather(gathered_day[:, 0:1, :], "row", axis=1, tiled=True).reshape(
            panel_size, panel_size
        )
        factor = jnp.linalg.cholesky(diagonal_full)
        inverse = lower_inverse(factor)
        owned = product(inverse, gathered_day.reshape(panel_size, remain * row_width)).reshape(
            panel_size, remain, row_width
        )
        if remain > 1:
            later = lax.all_gather(owned[:, 1:, None, :], "row", axis=2, tiled=True).reshape(
                panel_size, (remain - 1) * panel_size
            )
        solved_left = product(inverse, left_full[current])
        solved_right = product(inverse, right_full[current])
        solved_arrow = product(inverse, arrow_full[current])
        left_solved.append(solved_left)
        right_solved.append(solved_right)
        arrow_solved.append(solved_arrow)
        right_term = right_term + product_tn(own_columns(solved_right), solved_right)
        left_term = left_term + product_tn(own_columns(solved_left), solved_left)
        arrow_term = arrow_term + product_tn(solved_arrow, solved_arrow)
        mine_rows = lax.dynamic_slice_in_dim(owned, col_index * col_width, col_width, 0)
        diagonal_part = jnp.where(cols_at >= rows_at, mine_rows[:, 0, :], 0.0)
        factor_blocks.append(
            jnp.concatenate(
                [
                    jnp.zeros((col_width, current, row_width), jnp.float32),
                    diagonal_part[:, None, :],
                    mine_rows[:, 1:, :],
                ],
                axis=1,
            )
        )
        if remain > 1:
            mine_later = lax.dynamic_slice_in_dim(
                later.reshape(panel_size, remain - 1, panel_size), col_index * col_width, col_width, 2
            )
            mine_later = mine_later.reshape(panel_size, (remain - 1) * col_width).T
            owned_later = owned[:, 1:, :].reshape(panel_size, (remain - 1) * row_width)
            matrix = matrix.at[current + 1 :, :, current + 1 :, :].add(
                -product(mine_later, owned_later).reshape(
                    remain - 1, col_width, remain - 1, row_width
                )
            )
            left_update = product_tn(later, solved_left)
            right_update = product_tn(later, solved_right)
            arrow_update = product_tn(later, solved_arrow)
            for step in range(remain - 1):
                rows = slice(step * panel_size, (step + 1) * panel_size)
                left_full[current + 1 + step] = left_full[current + 1 + step] - left_update[rows]
                right_full[current + 1 + step] = right_full[current + 1 + step] - right_update[rows]
                arrow_full[current + 1 + step] = arrow_full[current + 1 + step] - arrow_update[rows]
    day_factor = jnp.stack(factor_blocks).reshape(day_block.shape)

    def mine(parts, width):
        whole = jnp.stack(parts).reshape(panels, col_count, col_width, width)
        return lax.dynamic_index_in_dim(whole, col_index, 1, keepdims=False)

    left_out = mine(left_solved, panels * row_width)
    right_out = mine(right_solved, panels * row_width)
    arrow_out = mine(arrow_solved, arrow_rows)
    separator_local = separator_block.reshape(panels * col_width, panels * row_width)
    from_next = passed_along(left_term, "tm", -1)
    separator = separator_local - right_term - from_next
    arrow_total = jnp.sum(lax.all_gather(arrow_term, "tm", axis=0, tiled=False), axis=0)
    arrowhead = arrow_block - arrow_total
    return (
        day_factor,
        left_out.reshape(left_coupling.shape),
        right_out.reshape(right_coupling.shape),
        arrow_out.reshape(arrow_coupling.shape),
        separator.reshape(separator_block.shape),
        arrowhead,
    )


def solution(mesh):
    return jax.shard_map(
        per_device,
        mesh=mesh,
        in_specs=(
            P("tm", None, "col", None, None, "row", None),
            P("tm", None, "col", None, None, "row", None),
            P("tm", None, "col", None, None, "row", None),
            P("tm", None, "col", None, None, "row", None),
            P("tm", None, "col", None, None),
            P(),
        ),
        out_specs=(
            P("tm", None, "col", None, None, "row", None),
            P("tm", None, "col", None, None, "row", None),
            P("tm", None, "col", None, None, "row", None),
            P("tm", None, "col", None, None),
            P("tm", None, "col", None, None, "row", None),
            P(),
        ),
        check_vma=False,
    )
```

```python
import jax
import jax.numpy as jnp
from jax import lax
from jax.sharding import PartitionSpec as P


def passed_along(value, axis, steps):
    count = lax.axis_size(axis)
    initial, last = (max(0, -steps), min(count, count - steps))
    return lax.ppermute(value, axis, [(source, source + steps) for source in range(initial, last)])


def product(left, right):
    return jnp.dot(left, right, precision=lax.Precision.HIGHEST, preferred_element_type=jnp.float32)


def lower_inverse(factor):
    identity = jnp.eye(factor.shape[0], dtype=jnp.float32)
    return lax.linalg.triangular_solve(factor, identity, left_side=True, lower=True)


def reorder_nodes(whole, panels, col_width):
    count = whole.shape[0]
    col_count = lax.axis_size("col")
    spread = whole.reshape(count, panels, col_count, col_width)
    return jnp.transpose(spread, (2, 1, 3, 0)).reshape(col_count * panels * col_width, count)


def separator_term(solved, panels, col_width, row_width):
    whole = lax.all_gather(
        solved.reshape(solved.shape[0], panels, 1, row_width), "row", axis=2, tiled=True
    )
    ordered = reorder_nodes(whole, panels, col_width)
    return lax.psum_scatter(product(ordered, solved), "col", scatter_dimension=0, tiled=True)


def product_tn(left, right):
    return lax.dot_general(
        left,
        right,
        (((0,), (0,)), ((), ())),
        precision=lax.Precision.HIGHEST,
        preferred_element_type=jnp.float32,
    )


def per_device(
    day_block, left_coupling, right_coupling, separator_block, arrow_coupling, arrow_block
):
    panels = day_block.shape[1]
    col_width = day_block.shape[3]
    row_width = day_block.shape[6]
    col_count = lax.axis_size("col")
    row_count = lax.axis_size("row")
    panel_size = col_width * col_count
    arrow_rows = arrow_block.shape[0]
    col_index = lax.axis_index("col")
    row_index = lax.axis_index("row")
    matrix = day_block.reshape(panels, col_width, panels, row_width)
    left_part = left_coupling.reshape(panels, col_width, panels * row_width)
    right_part = right_coupling.reshape(panels, col_width, panels * row_width)
    arrow_part = arrow_coupling.reshape(panels, col_width, arrow_rows)
    block_rows = []
    for k in range(panels):
        remain = panels - k
        by_col = lax.all_gather(matrix[k, :, k:, :], "col", axis=0, tiled=True)
        whole = lax.all_gather(by_col[:, :, None, :], "row", axis=2, tiled=True)
        block_rows.append(whole.reshape(panel_size, remain * panel_size))
    left_full = [lax.all_gather(left_part[k], "col", axis=0, tiled=True) for k in range(panels)]
    right_full = [lax.all_gather(right_part[k], "col", axis=0, tiled=True) for k in range(panels)]
    arrow_all = lax.all_gather(arrow_part, "col", axis=1, tiled=True)
    arrow_full = [arrow_all[k] for k in range(panels)]
    rows_at = col_index * col_width + lax.broadcasted_iota(jnp.int32, (col_width, row_width), 0)
    cols_at = row_index * row_width + lax.broadcasted_iota(jnp.int32, (col_width, row_width), 1)
    per_slice = row_width // col_width
    owner = col_index // per_slice
    offset = (col_index % per_slice) * col_width

    def own_columns(solved):
        spread = solved.reshape(panel_size, panels, row_width)
        picked = lax.dynamic_slice_in_dim(spread, offset, col_width, 2)
        picked = jnp.where(row_index == owner, picked, 0.0)
        return lax.psum(picked, "row").reshape(panel_size, panels * col_width)

    factor_blocks = []
    left_solved = []
    right_solved = []
    arrow_solved = []
    right_term = jnp.zeros((panels * col_width, panels * row_width), jnp.float32)
    left_term = jnp.zeros((panels * col_width, panels * row_width), jnp.float32)
    arrow_term = jnp.zeros((arrow_rows, arrow_rows), jnp.float32)
    for current in range(panels):
        remain = panels - current
        block_row = block_rows[current]
        diagonal_full = block_row[:, :panel_size]
        factor = jnp.linalg.cholesky(diagonal_full)
        inverse = lower_inverse(factor)
        owned_full = product(inverse, block_row)
        owned = lax.dynamic_slice_in_dim(
            owned_full.reshape(panel_size, remain, row_count, row_width), row_index, 1, 2
        ).reshape(panel_size, remain, row_width)
        solved_left = product(inverse, left_full[current])
        solved_right = product(inverse, right_full[current])
        solved_arrow = product(inverse, arrow_full[current])
        left_solved.append(solved_left)
        right_solved.append(solved_right)
        arrow_solved.append(solved_arrow)
        right_term = right_term + product_tn(own_columns(solved_right), solved_right)
        left_term = left_term + product_tn(own_columns(solved_left), solved_left)
        arrow_term = arrow_term + product_tn(solved_arrow, solved_arrow)
        mine_rows = lax.dynamic_slice_in_dim(owned, col_index * col_width, col_width, 0)
        diagonal_part = jnp.where(cols_at >= rows_at, mine_rows[:, 0, :], 0.0)
        factor_blocks.append(
            jnp.concatenate(
                [
                    jnp.zeros((col_width, current, row_width), jnp.float32),
                    diagonal_part[:, None, :],
                    mine_rows[:, 1:, :],
                ],
                axis=1,
            )
        )
        if remain > 1:
            later = owned_full[:, panel_size:]
            for step in range(remain - 1):
                target = current + 1 + step
                rows = slice(step * panel_size, (step + 1) * panel_size)
                block_rows[target] = block_rows[target] - product_tn(
                    later[:, rows], later[:, step * panel_size :]
                )
            left_update = product_tn(later, solved_left)
            right_update = product_tn(later, solved_right)
            arrow_update = product_tn(later, solved_arrow)
            for step in range(remain - 1):
                rows = slice(step * panel_size, (step + 1) * panel_size)
                left_full[current + 1 + step] = left_full[current + 1 + step] - left_update[rows]
                right_full[current + 1 + step] = right_full[current + 1 + step] - right_update[rows]
                arrow_full[current + 1 + step] = arrow_full[current + 1 + step] - arrow_update[rows]
    day_factor = jnp.stack(factor_blocks).reshape(day_block.shape)

    def mine(parts, width):
        whole = jnp.stack(parts).reshape(panels, col_count, col_width, width)
        return lax.dynamic_index_in_dim(whole, col_index, 1, keepdims=False)

    left_out = mine(left_solved, panels * row_width)
    right_out = mine(right_solved, panels * row_width)
    arrow_out = mine(arrow_solved, arrow_rows)
    separator_local = separator_block.reshape(panels * col_width, panels * row_width)
    from_next = passed_along(left_term, "tm", -1)
    separator = separator_local - right_term - from_next
    arrow_total = jnp.sum(lax.all_gather(arrow_term, "tm", axis=0, tiled=False), axis=0)
    arrowhead = arrow_block - arrow_total
    return (
        day_factor,
        left_out.reshape(left_coupling.shape),
        right_out.reshape(right_coupling.shape),
        arrow_out.reshape(arrow_coupling.shape),
        separator.reshape(separator_block.shape),
        arrowhead,
    )


def solution(mesh):
    return jax.shard_map(
        per_device,
        mesh=mesh,
        in_specs=(
            P("tm", None, "col", None, None, "row", None),
            P("tm", None, "col", None, None, "row", None),
            P("tm", None, "col", None, None, "row", None),
            P("tm", None, "col", None, None, "row", None),
            P("tm", None, "col", None, None),
            P(),
        ),
        out_specs=(
            P("tm", None, "col", None, None, "row", None),
            P("tm", None, "col", None, None, "row", None),
            P("tm", None, "col", None, None, "row", None),
            P("tm", None, "col", None, None),
            P("tm", None, "col", None, None, "row", None),
            P(),
        ),
        check_vma=False,
    )
```

```python
import jax
import jax.numpy as jnp
from jax import lax
from jax.sharding import PartitionSpec as P


def passed_along(value, axis, steps):
    count = lax.axis_size(axis)
    initial, last = (max(0, -steps), min(count, count - steps))
    return lax.ppermute(value, axis, [(source, source + steps) for source in range(initial, last)])


def product(left, right):
    return jnp.dot(left, right, precision=lax.Precision.HIGHEST, preferred_element_type=jnp.float32)


def lower_inverse(factor):
    identity = jnp.eye(factor.shape[0], dtype=jnp.float32)
    return lax.linalg.triangular_solve(factor, identity, left_side=True, lower=True)


def reorder_nodes(whole, panels, col_width):
    count = whole.shape[0]
    col_count = lax.axis_size("col")
    spread = whole.reshape(count, panels, col_count, col_width)
    return jnp.transpose(spread, (2, 1, 3, 0)).reshape(col_count * panels * col_width, count)


def separator_term(solved, panels, col_width, row_width):
    whole = lax.all_gather(
        solved.reshape(solved.shape[0], panels, 1, row_width), "row", axis=2, tiled=True
    )
    ordered = reorder_nodes(whole, panels, col_width)
    return lax.psum_scatter(product(ordered, solved), "col", scatter_dimension=0, tiled=True)


def product_tn(left, right):
    return lax.dot_general(
        left,
        right,
        (((0,), (0,)), ((), ())),
        precision=lax.Precision.HIGHEST,
        preferred_element_type=jnp.float32,
    )


def per_device(
    day_block, left_coupling, right_coupling, separator_block, arrow_coupling, arrow_block
):
    panels = day_block.shape[1]
    col_width = day_block.shape[3]
    row_width = day_block.shape[6]
    col_count = lax.axis_size("col")
    row_count = lax.axis_size("row")
    panel_size = col_width * col_count
    arrow_rows = arrow_block.shape[0]
    col_index = lax.axis_index("col")
    row_index = lax.axis_index("row")
    matrix = day_block.reshape(panels, col_width, panels, row_width)
    left_part = left_coupling.reshape(panels, col_width, panels * row_width)
    right_part = right_coupling.reshape(panels, col_width, panels * row_width)
    arrow_part = arrow_coupling.reshape(panels, col_width, arrow_rows)
    def gather_block_row(k, after):
        piece = matrix[k, :, k:, :]
        if after is not None:
            piece, _ = lax.optimization_barrier((piece, after))
        by_col = lax.all_gather(piece, "col", axis=0, tiled=True)
        whole = lax.all_gather(by_col[:, :, None, :], "row", axis=2, tiled=True)
        return whole.reshape(panel_size, (panels - k) * panel_size)

    def gather_coupling(k, after):
        pieces = (left_part[k], right_part[k])
        if after is not None:
            pieces, _ = lax.optimization_barrier((pieces, after))
        return tuple(lax.all_gather(piece, "col", axis=0, tiled=True) for piece in pieces)

    block_rows = [gather_block_row(0, None)] + [None] * (panels - 1)
    left_full = [None] * panels
    right_full = [None] * panels
    left_full[0], right_full[0] = gather_coupling(0, None)
    arrow_all = lax.all_gather(arrow_part, "col", axis=1, tiled=True)
    arrow_full = [arrow_all[k] for k in range(panels)]
    pending = [[] for _ in range(panels)]
    pending_left = [[] for _ in range(panels)]
    pending_right = [[] for _ in range(panels)]
    rows_at = col_index * col_width + lax.broadcasted_iota(jnp.int32, (col_width, row_width), 0)
    cols_at = row_index * row_width + lax.broadcasted_iota(jnp.int32, (col_width, row_width), 1)
    per_slice = row_width // col_width
    owner = col_index // per_slice
    offset = (col_index % per_slice) * col_width

    def own_columns(solved):
        spread = solved.reshape(panel_size, panels, row_width)
        picked = lax.dynamic_slice_in_dim(spread, offset, col_width, 2)
        picked = jnp.where(row_index == owner, picked, 0.0)
        return lax.psum(picked, "row").reshape(panel_size, panels * col_width)

    factor_blocks = []
    left_solved = []
    right_solved = []
    arrow_solved = []
    right_term = jnp.zeros((panels * col_width, panels * row_width), jnp.float32)
    left_term = jnp.zeros((panels * col_width, panels * row_width), jnp.float32)
    arrow_term = jnp.zeros((arrow_rows, arrow_rows), jnp.float32)
    for current in range(panels):
        remain = panels - current
        block_row = block_rows[current]
        for update in pending[current]:
            block_row = block_row - update
        diagonal_full = block_row[:, :panel_size]
        factor = jnp.linalg.cholesky(diagonal_full)
        if remain > 1:
            block_rows[current + 1] = gather_block_row(current + 1, factor)
            fresh_left, fresh_right = gather_coupling(current + 1, factor)
            for update in pending_left[current + 1]:
                fresh_left = fresh_left - update
            for update in pending_right[current + 1]:
                fresh_right = fresh_right - update
            left_full[current + 1], right_full[current + 1] = fresh_left, fresh_right
        inverse = lower_inverse(factor)
        owned_full = product(inverse, block_row)
        owned = lax.dynamic_slice_in_dim(
            owned_full.reshape(panel_size, remain, row_count, row_width), row_index, 1, 2
        ).reshape(panel_size, remain, row_width)
        solved_left = product(inverse, left_full[current])
        solved_right = product(inverse, right_full[current])
        solved_arrow = product(inverse, arrow_full[current])
        left_solved.append(solved_left)
        right_solved.append(solved_right)
        arrow_solved.append(solved_arrow)
        right_term = right_term + product_tn(own_columns(solved_right), solved_right)
        left_term = left_term + product_tn(own_columns(solved_left), solved_left)
        arrow_term = arrow_term + product_tn(solved_arrow, solved_arrow)
        mine_rows = lax.dynamic_slice_in_dim(owned, col_index * col_width, col_width, 0)
        diagonal_part = jnp.where(cols_at >= rows_at, mine_rows[:, 0, :], 0.0)
        factor_blocks.append(
            jnp.concatenate(
                [
                    jnp.zeros((col_width, current, row_width), jnp.float32),
                    diagonal_part[:, None, :],
                    mine_rows[:, 1:, :],
                ],
                axis=1,
            )
        )
        if remain > 1:
            later = owned_full[:, panel_size:]
            for step in range(remain - 1):
                target = current + 1 + step
                rows = slice(step * panel_size, (step + 1) * panel_size)
                pending[target].append(product_tn(later[:, rows], later[:, step * panel_size :]))
            left_update = product_tn(later, solved_left)
            right_update = product_tn(later, solved_right)
            arrow_update = product_tn(later, solved_arrow)
            for step in range(remain - 1):
                rows = slice(step * panel_size, (step + 1) * panel_size)
                target = current + 1 + step
                if step == 0:
                    left_full[target] = left_full[target] - left_update[rows]
                    right_full[target] = right_full[target] - right_update[rows]
                else:
                    pending_left[target].append(left_update[rows])
                    pending_right[target].append(right_update[rows])
                arrow_full[target] = arrow_full[target] - arrow_update[rows]
    day_factor = jnp.stack(factor_blocks).reshape(day_block.shape)

    def mine(parts, width):
        whole = jnp.stack(parts).reshape(panels, col_count, col_width, width)
        return lax.dynamic_index_in_dim(whole, col_index, 1, keepdims=False)

    left_out = mine(left_solved, panels * row_width)
    right_out = mine(right_solved, panels * row_width)
    arrow_out = mine(arrow_solved, arrow_rows)
    separator_local = separator_block.reshape(panels * col_width, panels * row_width)
    from_next = passed_along(left_term, "tm", -1)
    separator = separator_local - right_term - from_next
    arrow_total = jnp.sum(lax.all_gather(arrow_term, "tm", axis=0, tiled=False), axis=0)
    arrowhead = arrow_block - arrow_total
    return (
        day_factor,
        left_out.reshape(left_coupling.shape),
        right_out.reshape(right_coupling.shape),
        arrow_out.reshape(arrow_coupling.shape),
        separator.reshape(separator_block.shape),
        arrowhead,
    )


def solution(mesh):
    return jax.shard_map(
        per_device,
        mesh=mesh,
        in_specs=(
            P("tm", None, "col", None, None, "row", None),
            P("tm", None, "col", None, None, "row", None),
            P("tm", None, "col", None, None, "row", None),
            P("tm", None, "col", None, None, "row", None),
            P("tm", None, "col", None, None),
            P(),
        ),
        out_specs=(
            P("tm", None, "col", None, None, "row", None),
            P("tm", None, "col", None, None, "row", None),
            P("tm", None, "col", None, None, "row", None),
            P("tm", None, "col", None, None),
            P("tm", None, "col", None, None, "row", None),
            P(),
        ),
        check_vma=False,
    )
```

```python
import jax
import jax.numpy as jnp
from jax import lax
from jax.sharding import PartitionSpec as P


def passed_along(value, axis, steps):
    count = lax.axis_size(axis)
    initial, last = (max(0, -steps), min(count, count - steps))
    return lax.ppermute(value, axis, [(source, source + steps) for source in range(initial, last)])


def product(left, right):
    return jnp.dot(left, right, precision=lax.Precision.HIGHEST, preferred_element_type=jnp.float32)


def lower_inverse(factor):
    identity = jnp.eye(factor.shape[0], dtype=jnp.float32)
    return lax.linalg.triangular_solve(factor, identity, left_side=True, lower=True)


def reorder_nodes(whole, panels, col_width):
    count = whole.shape[0]
    col_count = lax.axis_size("col")
    spread = whole.reshape(count, panels, col_count, col_width)
    return jnp.transpose(spread, (2, 1, 3, 0)).reshape(col_count * panels * col_width, count)


def separator_term(solved, panels, col_width, row_width):
    whole = lax.all_gather(
        solved.reshape(solved.shape[0], panels, 1, row_width), "row", axis=2, tiled=True
    )
    ordered = reorder_nodes(whole, panels, col_width)
    return lax.psum_scatter(product(ordered, solved), "col", scatter_dimension=0, tiled=True)


def product_tn(left, right):
    return lax.dot_general(
        left,
        right,
        (((0,), (0,)), ((), ())),
        precision=lax.Precision.HIGHEST,
        preferred_element_type=jnp.float32,
    )


def per_device(
    day_block, left_coupling, right_coupling, separator_block, arrow_coupling, arrow_block
):
    panels = day_block.shape[1]
    col_width = day_block.shape[3]
    row_width = day_block.shape[6]
    col_count = lax.axis_size("col")
    row_count = lax.axis_size("row")
    panel_size = col_width * col_count
    arrow_rows = arrow_block.shape[0]
    col_index = lax.axis_index("col")
    row_index = lax.axis_index("row")
    matrix = day_block.reshape(panels, col_width, panels, row_width)
    left_part = left_coupling.reshape(panels, col_width, panels * row_width)
    right_part = right_coupling.reshape(panels, col_width, panels * row_width)
    arrow_part = arrow_coupling.reshape(panels, col_width, arrow_rows)
    day_width = lambda k: (panels - k) * row_width
    wide = panels * row_width

    def gather_panel(k, after):
        pieces = [left_part[k], right_part[k], arrow_part[k]]
        if k > 0:
            pieces = [matrix[k, :, k:, :].reshape(col_width, day_width(k))] + pieces
        if after is not None:
            pieces, _ = lax.optimization_barrier((pieces, after))
        joined = lax.all_gather(jnp.concatenate(pieces, axis=1), "col", axis=0, tiled=True)
        start = day_width(k) if k > 0 else 0
        left_new = joined[:, start : start + wide]
        right_new = joined[:, start + wide : start + 2 * wide]
        arrow_new = joined[:, start + 2 * wide :]
        if k == 0:
            return None, left_new, right_new, arrow_new
        by_col = joined[:, :start].reshape(panel_size, panels - k, row_width)
        whole = lax.all_gather(by_col[:, :, None, :], "row", axis=2, tiled=True)
        return whole.reshape(panel_size, (panels - k) * panel_size), left_new, right_new, arrow_new

    first_col = lax.all_gather(matrix[0], "col", axis=0, tiled=True)
    first_row = lax.all_gather(first_col[:, :, None, :], "row", axis=2, tiled=True)
    block_rows = [first_row.reshape(panel_size, panels * panel_size)] + [None] * (panels - 1)
    left_full = [None] * panels
    right_full = [None] * panels
    arrow_full = [None] * panels
    _, left_full[0], right_full[0], arrow_full[0] = gather_panel(0, None)
    pending = [[] for _ in range(panels)]
    pending_left = [[] for _ in range(panels)]
    pending_right = [[] for _ in range(panels)]
    pending_arrow = [[] for _ in range(panels)]
    rows_at = col_index * col_width + lax.broadcasted_iota(jnp.int32, (col_width, row_width), 0)
    cols_at = row_index * row_width + lax.broadcasted_iota(jnp.int32, (col_width, row_width), 1)
    per_slice = row_width // col_width
    owner = col_index // per_slice
    offset = (col_index % per_slice) * col_width

    def own_columns(solved_pair, after):
        picked = []
        for solved in solved_pair:
            spread = solved.reshape(panel_size, panels, row_width)
            part = lax.dynamic_slice_in_dim(spread, offset, col_width, 2)
            picked.append(jnp.where(row_index == owner, part, 0.0))
        if after is not None:
            picked, _ = lax.optimization_barrier((picked, after))
        summed = lax.psum(picked, "row")
        return [part.reshape(panel_size, panels * col_width) for part in summed]

    previous_sum = None

    factor_blocks = []
    left_solved = []
    right_solved = []
    arrow_solved = []
    right_term = jnp.zeros((panels * col_width, panels * row_width), jnp.float32)
    left_term = jnp.zeros((panels * col_width, panels * row_width), jnp.float32)
    arrow_term = jnp.zeros((arrow_rows, arrow_rows), jnp.float32)
    for current in range(panels):
        remain = panels - current
        block_row = block_rows[current]
        for update in pending[current]:
            block_row = block_row - update
        diagonal_full = block_row[:, :panel_size]
        factor = jnp.linalg.cholesky(diagonal_full)
        if remain > 1:
            block_rows[current + 1], fresh_left, fresh_right, fresh_arrow = gather_panel(
                current + 1, factor
            )
            for update in pending_left[current + 1]:
                fresh_left = fresh_left - update
            for update in pending_right[current + 1]:
                fresh_right = fresh_right - update
            for update in pending_arrow[current + 1]:
                fresh_arrow = fresh_arrow - update
            left_full[current + 1] = fresh_left
            right_full[current + 1] = fresh_right
            arrow_full[current + 1] = fresh_arrow
        inverse = lower_inverse(factor)
        owned_full = product(inverse, block_row)
        owned = lax.dynamic_slice_in_dim(
            owned_full.reshape(panel_size, remain, row_count, row_width), row_index, 1, 2
        ).reshape(panel_size, remain, row_width)
        solved_left = product(inverse, left_full[current])
        solved_right = product(inverse, right_full[current])
        solved_arrow = product(inverse, arrow_full[current])
        left_solved.append(solved_left)
        right_solved.append(solved_right)
        arrow_solved.append(solved_arrow)
        own_right, own_left = own_columns((solved_right, solved_left), previous_sum)
        previous_sum = own_left
        right_term = right_term + product_tn(own_right, solved_right)
        left_term = left_term + product_tn(own_left, solved_left)
        arrow_term = arrow_term + product_tn(solved_arrow, solved_arrow)
        mine_rows = lax.dynamic_slice_in_dim(owned, col_index * col_width, col_width, 0)
        diagonal_part = jnp.where(cols_at >= rows_at, mine_rows[:, 0, :], 0.0)
        factor_blocks.append(
            jnp.concatenate(
                [
                    jnp.zeros((col_width, current, row_width), jnp.float32),
                    diagonal_part[:, None, :],
                    mine_rows[:, 1:, :],
                ],
                axis=1,
            )
        )
        if remain > 1:
            later = owned_full[:, panel_size:]
            for step in range(remain - 1):
                target = current + 1 + step
                rows = slice(step * panel_size, (step + 1) * panel_size)
                pending[target].append(product_tn(later[:, rows], later[:, step * panel_size :]))
            left_update = product_tn(later, solved_left)
            right_update = product_tn(later, solved_right)
            arrow_update = product_tn(later, solved_arrow)
            for step in range(remain - 1):
                rows = slice(step * panel_size, (step + 1) * panel_size)
                target = current + 1 + step
                if step == 0:
                    left_full[target] = left_full[target] - left_update[rows]
                    right_full[target] = right_full[target] - right_update[rows]
                    arrow_full[target] = arrow_full[target] - arrow_update[rows]
                else:
                    pending_left[target].append(left_update[rows])
                    pending_right[target].append(right_update[rows])
                    pending_arrow[target].append(arrow_update[rows])
    day_factor = jnp.stack(factor_blocks).reshape(day_block.shape)

    def mine(parts, width):
        whole = jnp.stack(parts).reshape(panels, col_count, col_width, width)
        return lax.dynamic_index_in_dim(whole, col_index, 1, keepdims=False)

    left_out = mine(left_solved, panels * row_width)
    right_out = mine(right_solved, panels * row_width)
    arrow_out = mine(arrow_solved, arrow_rows)
    separator_local = separator_block.reshape(panels * col_width, panels * row_width)
    from_next = passed_along(left_term, "tm", -1)
    separator = separator_local - right_term - from_next
    arrow_total = jnp.sum(lax.all_gather(arrow_term, "tm", axis=0, tiled=False), axis=0)
    arrowhead = arrow_block - arrow_total
    return (
        day_factor,
        left_out.reshape(left_coupling.shape),
        right_out.reshape(right_coupling.shape),
        arrow_out.reshape(arrow_coupling.shape),
        separator.reshape(separator_block.shape),
        arrowhead,
    )


def solution(mesh):
    return jax.shard_map(
        per_device,
        mesh=mesh,
        in_specs=(
            P("tm", None, "col", None, None, "row", None),
            P("tm", None, "col", None, None, "row", None),
            P("tm", None, "col", None, None, "row", None),
            P("tm", None, "col", None, None, "row", None),
            P("tm", None, "col", None, None),
            P(),
        ),
        out_specs=(
            P("tm", None, "col", None, None, "row", None),
            P("tm", None, "col", None, None, "row", None),
            P("tm", None, "col", None, None, "row", None),
            P("tm", None, "col", None, None),
            P("tm", None, "col", None, None, "row", None),
            P(),
        ),
        check_vma=False,
    )
```
